32 devices in a mesh: parts: 2 (over y), req: 8 (over z, x), mp: 2 (over core).
Axes of the slice: x: 2, y: 2, z: 4, core: 2. Of those that a mesh axis runs over, the one named last changes fastest.
Arguments:
- hidden: bfloat16 [2048, 8192], P(('parts', 'req'), 'mp'), parts along dimension 0, may hold values from -6 to 6
- base_query_block: bfloat16 [2048, 1024], P(('parts', 'req'), 'mp'), parts along dimension 0, may hold values from -112 to 112
- key_value_block: bfloat16 [2048, 256], P(('parts', 'req')), parts along dimension 0, may hold values from -7.1875 to 7.1875
- prefix_page_store: bfloat16 [256, 32, 256], P(('parts', 'req')), parts along dimension 0, may hold values from -8 to 8
- adapter_down_weight: bfloat16 [8, 2, 64, 4096], P('req', 'mp'), may hold values from -0.0625 to 0.0625
- adapter_up_weight: bfloat16 [8, 2, 64, 512], P('req', 'mp'), may hold values from -0.75 to 0.75
- request_adapter: int32 [16], P(('parts', 'req')), parts along dimension 0, may hold values from 0 to 7
- prefix_page_count: int32 [16], P(('parts', 'req')), parts along dimension 0, may hold values from 2 to 8, as said below
- page_owner_groups: int32 [16, 8], P(('parts', 'req')), parts along dimension 0, may hold values from 0 to 7, as said below
- page_pool_row: int32 [16, 8], P(('parts', 'req')), parts along dimension 0, may hold values from 0 to 15
Outputs:
- attn_out: bfloat16 [2048, 1024], P(('parts', 'req'), 'mp'), parts along dimension 0
The draws below stay inside these ranges and needn't reach their ends.
There are 2 independent parts, one for each index of `parts`. The reference program is written for one: setup_inputs(seed, part) draws one part's arguments, and reference() takes and returns one part's arrays. A program takes and returns all parts, laid end to end along the dimension named above; an argument that names none is the same for every part. Nothing has to cross between parts.
Inputs may be any that keep to these rules, and one draw needn't show every extreme that they name: `prefix_page_count`: some request has exactly 8 prefix pages. `page_owner_groups`: each row names every request group once; its first prefix_page_count[r] entries hold request r's prefix pages, the rest is padding.
All inputs are finite; a program needn't handle non-finite values.
Results may differ from the reference program's by a relative error of at most 0.025.
Values may be sent and summed in bfloat16 or wider, within the bound.
No kernel may reach another device: no remote copies, remote signals or barrier semaphores. Data moves between devices by JAX's collectives and lax.ppermute only.
A program may use at most 64 MiB of HBM per device.

```python
import math
import jax
import jax.numpy as jnp
import numpy as np
from jax import lax

MODEL_WIDTH = 8192
GROUP_HEADS = 8
HEAD_SIZE = 128
ADAPTER_RANK = 64
BLOCK_TOKENS = 128
PAGE = 32
POOL = 16
ADAPTER_COUNT = 8
REQS = 8
MAXP = 8
POOLS = 128
TOKENS = 1024
N_MP = 2


def draw_base_query_block(key, part):
    array_shape = (TOKENS, GROUP_HEADS * HEAD_SIZE)
    entries = jax.random.normal(jax.random.fold_in(key, 3), array_shape, jnp.float32) * 2.0
    return jnp.clip(entries, -12.0, 12.0).astype(jnp.bfloat16)


def draw_prefix_page_store(key, part):
    key_part = jnp.clip(jax.random.normal(jax.random.fold_in(key, 3), (POOLS, PAGE, HEAD_SIZE), jnp.float32) * 1.2, -7.2, 7.2)
    value_part = jnp.clip(jax.random.normal(jax.random.fold_in(key, 4), (POOLS, PAGE, HEAD_SIZE), jnp.float32) * 1.2, -7.2, 7.2)
    return jnp.concatenate([key_part, value_part], axis=2).astype(jnp.bfloat16)


def draw_prefix_page_count(key, part):
    counts = jax.random.randint(jax.random.fold_in(key, 1), (REQS,), max(1, MAXP // 4), MAXP + 1)
    full_row = jax.random.randint(jax.random.fold_in(key, 2), (), 0, REQS)
    return jnp.where(jnp.arange(REQS) == full_row, MAXP, counts).astype(jnp.int32)


def draw_page_owner_groups(key, part):
    row_keys = jax.random.split(jax.random.fold_in(key, 5), REQS)
    return jax.vmap(lambda subkey: jax.random.permutation(subkey, MAXP))(row_keys).astype(jnp.int32)


def place_ends(values, stream_key, smallest, high):
    extent = values.shape
    index_at = [jax.random.randint(jax.random.fold_in(stream_key, axis), (), 0, extent[axis]) for axis in range(len(extent))]
    values = values.at[tuple(index_at)].set(smallest)
    longest = extent.index(max(extent))
    index_at[longest] = (index_at[longest] + 1) % extent[longest]
    return values.at[tuple(index_at)].set(high)


def steps_of(own_key, extent, cuts, smallest, largest):
    loudness = 1.0
    for dim, parts in cuts:
        steps = jax.random.uniform(jax.random.fold_in(jax.random.fold_in(own_key, 6), dim), (parts,), jnp.float32, smallest / len(cuts), largest / len(cuts))
        loudness = loudness * jnp.repeat(jnp.exp(steps), extent[dim] // parts).reshape((-1,) + (1,) * (len(extent) - 1 - dim))
    return loudness


def rank_table(number_of, lean):
    loads = [(1 << 20) // math.isqrt(grade ** lean) + 1 for grade in range(1, number_of + 1)]
    deviation = 1 + sum(loads) // (1 << 30)
    return np.cumsum(np.array([max(1, weight // deviation) for weight in loads]))


def ranked_ids(key, extent, count, slope):
    listing = rank_table(count, slope)
    lot = jax.random.randint(jax.random.fold_in(key, 1), extent, 0, int(listing[count - 1]))
    rank = jnp.searchsorted(jnp.asarray(listing, jnp.int32), lot, side="right")
    return jax.random.permutation(jax.random.fold_in(key, 2), count)[rank].astype(jnp.int32)


def normal_values(stream_key, shape, deviation, most, shards=(), kind=jnp.bfloat16):
    drawn = deviation * jax.random.normal(stream_key, shape, jnp.float32)
    if shards:
        drawn = drawn * steps_of(stream_key, shape, shards, -0.22, 0.18)
    return jnp.clip(drawn, -most, most).astype(kind)


def setup_inputs(seed: int = 0, part: int = 0) -> dict:
    arg_keys = jax.random.split(jax.random.key(seed), 11)
    part_splits = jax.random.split(jax.random.fold_in(arg_keys[10], part), 11)
    return {
        "hidden": normal_values(part_splits[0], (TOKENS, MODEL_WIDTH), 1.0, 6.0, ((0, 8), (1, 2))),
        "base_query_block": draw_base_query_block(jax.random.fold_in(jax.random.fold_in(arg_keys[10], part), 71), part),
        "key_value_block": normal_values(part_splits[2], (TOKENS, 2 * HEAD_SIZE), 1.2, 7.1875, ((0, 8),)),
        "prefix_page_store": draw_prefix_page_store(jax.random.fold_in(jax.random.fold_in(arg_keys[10], part), 71), part),
        "adapter_down_weight": normal_values(arg_keys[4], (ADAPTER_COUNT, N_MP, ADAPTER_RANK, MODEL_WIDTH // N_MP), MODEL_WIDTH ** -0.5, 0.0625, ((0, 8), (1, 2))),
        "adapter_up_weight": normal_values(arg_keys[5], (ADAPTER_COUNT, N_MP, ADAPTER_RANK, GROUP_HEADS * HEAD_SIZE // N_MP), ADAPTER_RANK ** -0.5, 0.75, ((0, 8), (1, 2))),
        "request_adapter": place_ends(ranked_ids(part_splits[6], (REQS,), ADAPTER_COUNT, 2), jax.random.fold_in(part_splits[6], 3), 0, ADAPTER_COUNT - 1).astype(jnp.int32),
        "prefix_page_count": draw_prefix_page_count(jax.random.fold_in(jax.random.fold_in(arg_keys[10], part), 71), part),
        "page_owner_groups": draw_page_owner_groups(jax.random.fold_in(jax.random.fold_in(arg_keys[10], part), 71), part),
        "page_pool_row": place_ends(jax.random.randint(part_splits[9], (REQS, MAXP), 0, POOL), jax.random.fold_in(part_splits[9], 1), 0, POOL - 1).astype(jnp.int32),
    }


ROPE_BASE = 500000.0

def rotate(vectors, positions):
    head_width = vectors.shape[-1]
    half_dim = head_width // 2
    frequency = ROPE_BASE ** (-2.0 * jnp.arange(half_dim, dtype=jnp.float32) / head_width)
    angles = positions.astype(jnp.float32)[:, None] * frequency[None, :]
    cosine = jnp.concatenate([jnp.cos(angles), jnp.cos(angles)], axis=1)[:, None, :]
    sine_part = jnp.concatenate([jnp.sin(angles), jnp.sin(angles)], axis=1)[:, None, :]
    turned = jnp.concatenate([-vectors[..., half_dim:], vectors[..., :half_dim]], axis=-1)
    return vectors * cosine + turned * sine_part

def attend(queries, all_keys, all_values, allowed):
    score_scale = 1.0 / math.sqrt(all_keys.shape[1])

    def one_head(query_rows):
        scores = lax.dot_general(query_rows, all_keys, (((1,), (1,)), ((), ())), preferred_element_type=jnp.float32) * score_scale
        scores = jnp.where(allowed, scores, -jnp.inf)
        row_max = lax.optimization_barrier(jnp.max(scores, axis=1, keepdims=True))
        weights = jnp.exp(scores - row_max)
        weights_bf = (weights / lax.optimization_barrier(jnp.sum(weights, axis=1, keepdims=True))).astype(jnp.bfloat16)
        return jnp.dot(weights_bf, all_values, preferred_element_type=jnp.float32).astype(jnp.bfloat16)
    outputs = lax.map(one_head, jnp.moveaxis(queries, 1, 0))
    return jnp.moveaxis(outputs, 0, 1).reshape(queries.shape[0], -1)

def reference(hidden, base_query_block, key_value_block, prefix_page_store, adapter_down_weight, adapter_up_weight, request_adapter, prefix_page_count, page_owner_groups, page_pool_row):

    def one_request(request_items):
        token_rows, base_query_rows, block_kv, adapter_weights, page_count, holders, indices = request_items
        down_projected_rows = jnp.moveaxis(adapter_down_weight[adapter_weights], 0, 1).reshape(ADAPTER_RANK, MODEL_WIDTH)
        up_projected_rows = jnp.moveaxis(adapter_up_weight[adapter_weights], 0, 1).reshape(ADAPTER_RANK, GROUP_HEADS * HEAD_SIZE)
        rank_reduce = lax.dot_general(token_rows, down_projected_rows, (((1,), (1,)), ((), ())), preferred_element_type=jnp.float32).astype(jnp.bfloat16)
        adapter_delta = jnp.dot(rank_reduce, up_projected_rows, preferred_element_type=jnp.float32)
        positions = PAGE * page_count + jnp.arange(BLOCK_TOKENS, dtype=jnp.int32)
        reduced_sum = (base_query_rows.astype(jnp.float32) + adapter_delta).reshape(BLOCK_TOKENS, GROUP_HEADS, HEAD_SIZE)
        queries = rotate(reduced_sum, positions).astype(jnp.bfloat16)
        block_keys = rotate(block_kv[:, None, :HEAD_SIZE].astype(jnp.float32), positions)[:, 0].astype(jnp.bfloat16)
        rows_wanted = (holders * POOL + indices).astype(jnp.int32)
        fetched = prefix_page_store[rows_wanted].reshape(MAXP * PAGE, 2 * HEAD_SIZE)
        live_slots = jnp.repeat(jnp.arange(MAXP, dtype=jnp.int32) < page_count, PAGE)
        all_keys = jnp.concatenate([fetched[:, :HEAD_SIZE], block_keys], axis=0)
        all_values = jnp.concatenate([fetched[:, HEAD_SIZE:], block_kv[:, HEAD_SIZE:]], axis=0)
        token_order = jnp.arange(BLOCK_TOKENS, dtype=jnp.int32)
        causal = token_order[:, None] >= token_order[None, :]
        allowed = jnp.concatenate([jnp.broadcast_to(live_slots[None, :], (BLOCK_TOKENS, MAXP * PAGE)), causal], axis=1)
        return attend(queries, all_keys, all_values, allowed)
    outputs = lax.map(one_request, (hidden.reshape(REQS, BLOCK_TOKENS, MODEL_WIDTH), base_query_block.reshape(REQS, BLOCK_TOKENS, GROUP_HEADS * HEAD_SIZE), key_value_block.reshape(REQS, BLOCK_TOKENS, 2 * HEAD_SIZE), request_adapter, prefix_page_count, page_owner_groups, page_pool_row))
    return outputs.reshape(TOKENS, GROUP_HEADS * HEAD_SIZE)
```

```python
import math

import jax
import jax.numpy as jnp
from jax import lax
from jax.sharding import PartitionSpec as P

ROPE_BASE = 500000.0
LANES = 128
TILE_ROWS = 16


def rotate(vectors, positions):
    head_width = vectors.shape[-1]
    half_dim = head_width // 2
    frequency = ROPE_BASE ** (-2.0 * jnp.arange(half_dim, dtype=jnp.float32) / head_width)
    angles = positions.astype(jnp.float32)[:, None] * frequency[None, :]
    cosine = jnp.concatenate([jnp.cos(angles), jnp.cos(angles)], axis=1)[:, None, :]
    sine_part = jnp.concatenate([jnp.sin(angles), jnp.sin(angles)], axis=1)[:, None, :]
    turned = jnp.concatenate([-vectors[..., half_dim:], vectors[..., :half_dim]], axis=-1)
    return vectors * cosine + turned * sine_part


def tiled_ok(shape, groups):
    rows, cols = shape
    if rows % TILE_ROWS or cols % LANES:
        return False
    return ((rows // TILE_ROWS) * (cols // LANES)) % groups == 0


def to_pieces(matrix, groups):
    rows, cols = matrix.shape
    if tiled_ok(matrix.shape, groups):
        tiles = matrix.reshape(rows // TILE_ROWS, TILE_ROWS, cols // LANES, LANES)
        tiles = jnp.transpose(tiles, (0, 2, 1, 3))
        return tiles.reshape(groups, -1, LANES)
    flat = matrix.reshape(groups, -1)
    extra = (-flat.shape[1]) % LANES
    if extra:
        flat = jnp.pad(flat, ((0, 0), (0, extra)))
    return flat.reshape(groups, -1, LANES)


def from_pieces(pieces, shape):
    rows, cols = shape
    groups = pieces.shape[0]
    if tiled_ok(shape, groups):
        tiles = pieces.reshape(rows // TILE_ROWS, cols // LANES, TILE_ROWS, LANES)
        tiles = jnp.transpose(tiles, (0, 2, 1, 3))
        return tiles.reshape(rows, cols)
    flat = pieces.reshape(groups, -1)[:, : rows * cols // groups]
    return flat.reshape(rows, cols)


def piece_rows(shape, groups):
    rows, cols = shape
    if tiled_ok(shape, groups):
        return rows * cols // groups // LANES
    return -(-(rows * cols // groups) // LANES)


def attend(queries, all_keys, all_values, allowed):
    token_count, head_count, head_width = queries.shape
    score_scale = 1.0 / math.sqrt(head_width)
    rows = queries.reshape(token_count * head_count, head_width)
    scores = (
        lax.dot_general(
            rows, all_keys, (((1,), (1,)), ((), ())), preferred_element_type=jnp.float32
        )
        * score_scale
    )
    scores = scores.reshape(token_count, head_count, -1)
    scores = jnp.where(allowed[:, None, :], scores, -jnp.inf)
    row_max = jnp.max(scores, axis=2, keepdims=True)
    weights = jnp.exp(scores - row_max)
    weights_bf = (weights / jnp.sum(weights, axis=2, keepdims=True)).astype(jnp.bfloat16)
    out = jnp.dot(
        weights_bf.reshape(token_count * head_count, -1),
        all_values,
        preferred_element_type=jnp.float32,
    ).astype(jnp.bfloat16)
    return out.reshape(token_count, head_count * head_width)


def on_device(
    hidden,
    base_query_block,
    key_value_block,
    prefix_page_store,
    adapter_down_weight,
    adapter_up_weight,
    request_adapter,
    prefix_page_count,
    page_owner_groups,
    page_pool_row,
):
    groups = lax.axis_size("req")
    head_width = key_value_block.shape[1] // 2
    total_row_count = hidden.shape[0]
    page_len = prefix_page_store.shape[1]
    held = adapter_down_weight.shape[0]
    down_shape = adapter_down_weight.shape[2:]
    up_shape = adapter_up_weight.shape[2:]
    down_rows = piece_rows(down_shape, groups)
    up_rows = piece_rows(up_shape, groups)

    page_count = prefix_page_count[0]
    slot_order = jnp.arange(page_owner_groups.shape[1], dtype=jnp.int32)
    live_slots = slot_order < page_count
    holder_order = jnp.arange(groups, dtype=jnp.int32)
    matched = (page_owner_groups[0][None, :] == holder_order[:, None]) & live_slots[None, :]
    wanted = jnp.max(jnp.where(matched, page_pool_row[0][None, :], -1), axis=1)

    asks = jnp.zeros((groups, 1, LANES), jnp.float32)
    asks = asks.at[:, 0, 0].set(jnp.maximum(wanted, 0).astype(jnp.float32))
    asks = asks.at[:, 0, 1].set(request_adapter[0].astype(jnp.float32))
    parts_out = []
    for a in range(held):
        parts_out.append(to_pieces(adapter_down_weight[a, 0], groups))
        parts_out.append(to_pieces(adapter_up_weight[a, 0], groups))
    parts_out.append(asks.astype(jnp.bfloat16))
    stage_one = jnp.concatenate(parts_out, axis=1)
    stage_one = lax.all_to_all(stage_one, "req", split_axis=0, concat_axis=0, tiled=True)

    share_rows = down_rows + up_rows
    shares = stage_one[:, : held * share_rows].reshape(groups * held, share_rows, LANES)
    their_asks = stage_one[:, held * share_rows, :2].astype(jnp.int32)
    their_pages = their_asks[:, 0]
    their_adapters = their_asks[:, 1]

    picked = jnp.take(shares, their_adapters, axis=0)
    pages = jnp.take(prefix_page_store, their_pages, axis=0)
    page_pieces = jax.vmap(lambda page: to_pieces(page, 1)[0])(pages)
    stage_two = jnp.concatenate([picked, page_pieces], axis=1)
    stage_two = lax.all_to_all(stage_two, "req", split_axis=0, concat_axis=0, tiled=True)

    down_projected_rows = from_pieces(stage_two[:, :down_rows], down_shape)
    up_projected_rows = from_pieces(stage_two[:, down_rows:share_rows], up_shape)
    fetched = jax.vmap(lambda piece: from_pieces(piece[None], (page_len, 2 * head_width)))(
        stage_two[:, share_rows:]
    )

    partial_value = lax.dot_general(
        hidden, down_projected_rows, (((1,), (1,)), ((), ())), preferred_element_type=jnp.float32
    )
    rank_reduce = lax.psum(partial_value, "mp").astype(jnp.bfloat16)
    adapter_delta = jnp.dot(rank_reduce, up_projected_rows, preferred_element_type=jnp.float32)
    query_head_count = base_query_block.shape[1] // head_width
    positions = page_len * page_count + jnp.arange(total_row_count, dtype=jnp.int32)
    reduced_sum = (base_query_block.astype(jnp.float32) + adapter_delta).reshape(
        total_row_count, query_head_count, head_width
    )
    queries = rotate(reduced_sum, positions).astype(jnp.bfloat16)
    block_keys = rotate(key_value_block[:, None, :head_width].astype(jnp.float32), positions)[
        :, 0
    ].astype(jnp.bfloat16)
    flat_pages = fetched.reshape(groups * page_len, 2 * head_width)
    prefix_mask = jnp.repeat(wanted >= 0, page_len)
    all_keys = jnp.concatenate([flat_pages[:, :head_width], block_keys], axis=0)
    all_values = jnp.concatenate(
        [flat_pages[:, head_width:], key_value_block[:, head_width:]], axis=0
    )
    token_order = jnp.arange(total_row_count, dtype=jnp.int32)
    causal = token_order[:, None] >= token_order[None, :]
    allowed = jnp.concatenate(
        [
            jnp.broadcast_to(prefix_mask[None, :], (total_row_count, groups * page_len)),
            causal,
        ],
        axis=1,
    )
    return attend(queries, all_keys, all_values, allowed)


def solution(mesh):
    in_specs = (
        P(("parts", "req"), "mp"),
        P(("parts", "req"), "mp"),
        P(("parts", "req"), None),
        P(("parts", "req"), None, None),
        P("req", "mp", None, None),
        P("req", "mp", None, None),
        P(("parts", "req")),
        P(("parts", "req")),
        P(("parts", "req"), None),
        P(("parts", "req"), None),
    )
    out_specs = P(("parts", "req"), "mp")
    return jax.shard_map(
        on_device, mesh=mesh, in_specs=in_specs, out_specs=out_specs, check_vma=False
    )
```

```python
import math

import jax
import jax.numpy as jnp
from jax import lax
from jax.sharding import PartitionSpec as P

ROPE_BASE = 500000.0
LANES = 128
TILE_ROWS = 8


def rotate(vectors, positions):
    head_width = vectors.shape[-1]
    half_dim = head_width // 2
    frequency = ROPE_BASE ** (-2.0 * jnp.arange(half_dim, dtype=jnp.float32) / head_width)
    angles = positions.astype(jnp.float32)[:, None] * frequency[None, :]
    cosine = jnp.concatenate([jnp.cos(angles), jnp.cos(angles)], axis=1)[:, None, :]
    sine_part = jnp.concatenate([jnp.sin(angles), jnp.sin(angles)], axis=1)[:, None, :]
    turned = jnp.concatenate([-vectors[..., half_dim:], vectors[..., :half_dim]], axis=-1)
    return vectors * cosine + turned * sine_part


def tiled_ok(shape, groups):
    rows, cols = shape
    if rows % TILE_ROWS or cols % LANES:
        return False
    return ((rows // TILE_ROWS) * (cols // LANES)) % groups == 0


def to_pieces(matrix, groups):
    rows, cols = matrix.shape
    if tiled_ok(matrix.shape, groups):
        tiles = matrix.reshape(rows // TILE_ROWS, TILE_ROWS, cols // LANES, LANES)
        tiles = jnp.transpose(tiles, (0, 2, 1, 3))
        return tiles.reshape(groups, -1, LANES)
    flat = matrix.reshape(groups, -1)
    extra = (-flat.shape[1]) % LANES
    if extra:
        flat = jnp.pad(flat, ((0, 0), (0, extra)))
    return flat.reshape(groups, -1, LANES)


def from_pieces(pieces, shape):
    rows, cols = shape
    groups = pieces.shape[0]
    if tiled_ok(shape, groups):
        tiles = pieces.reshape(rows // TILE_ROWS, cols // LANES, TILE_ROWS, LANES)
        tiles = jnp.transpose(tiles, (0, 2, 1, 3))
        return tiles.reshape(rows, cols)
    flat = pieces.reshape(groups, -1)[:, : rows * cols // groups]
    return flat.reshape(rows, cols)


def piece_rows(shape, groups):
    rows, cols = shape
    if tiled_ok(shape, groups):
        return rows * cols // groups // LANES
    return -(-(rows * cols // groups) // LANES)


def attend(queries, all_keys, all_values, allowed):
    token_count, head_count, head_width = queries.shape
    score_scale = 1.0 / math.sqrt(head_width)
    rows = queries.reshape(token_count * head_count, head_width)
    scores = (
        lax.dot_general(
            rows, all_keys, (((1,), (1,)), ((), ())), preferred_element_type=jnp.float32
        )
        * score_scale
    )
    scores = scores.reshape(token_count, head_count, -1)
    scores = jnp.where(allowed[:, None, :], scores, -jnp.inf)
    row_max = jnp.max(scores, axis=2, keepdims=True)
    weights = jnp.exp(scores - row_max)
    weights_bf = (weights / jnp.sum(weights, axis=2, keepdims=True)).astype(jnp.bfloat16)
    out = jnp.dot(
        weights_bf.reshape(token_count * head_count, -1),
        all_values,
        preferred_element_type=jnp.float32,
    ).astype(jnp.bfloat16)
    return out.reshape(token_count, head_count * head_width)


def on_device(
    hidden,
    base_query_block,
    key_value_block,
    prefix_page_store,
    adapter_down_weight,
    adapter_up_weight,
    request_adapter,
    prefix_page_count,
    page_owner_groups,
    page_pool_row,
):
    groups = lax.axis_size("req")
    head_width = key_value_block.shape[1] // 2
    total_row_count = hidden.shape[0]
    page_len = prefix_page_store.shape[1]
    held = adapter_down_weight.shape[0]
    down_shape = adapter_down_weight.shape[2:]
    up_shape = adapter_up_weight.shape[2:]
    down_rows = piece_rows(down_shape, groups)
    up_rows = piece_rows(up_shape, groups)

    page_count = prefix_page_count[0]
    slot_order = jnp.arange(page_owner_groups.shape[1], dtype=jnp.int32)
    live_slots = slot_order < page_count
    holder_order = jnp.arange(groups, dtype=jnp.int32)
    matched = (page_owner_groups[0][None, :] == holder_order[:, None]) & live_slots[None, :]
    wanted = jnp.max(jnp.where(matched, page_pool_row[0][None, :], -1), axis=1)

    page_shape = prefix_page_store.shape[1:]
    row_block = down_shape[0] // groups if down_shape[0] % groups == 0 else 0
    fast = (
        row_block > 0
        and row_block % TILE_ROWS == 0
        and up_shape[0] == down_shape[0]
        and (page_shape[0] * page_shape[1]) % (row_block * LANES) == 0
    )
    lane = lax.broadcasted_iota(jnp.int32, (groups, LANES), 1)
    asks = jnp.where(
        lane == 0,
        jnp.maximum(wanted, 0)[:, None],
        jnp.where(lane == 1, request_adapter[0], 0),
    ).astype(jnp.bfloat16)

    if fast:
        down_cols = down_shape[1]
        share_cols = down_cols + up_shape[1]
        ask_rows = jnp.broadcast_to(asks[:, None, :], (groups, row_block, LANES))
        parts_out = []
        for a in range(held):
            parts_out.append(adapter_down_weight[a, 0].reshape(groups, row_block, -1))
            parts_out.append(adapter_up_weight[a, 0].reshape(groups, row_block, -1))
        parts_out.append(ask_rows)
        stage_one = jnp.concatenate(parts_out, axis=2)
        stage_one = lax.all_to_all(stage_one, "req", split_axis=0, concat_axis=0, tiled=True)
        shares = stage_one[:, :, : held * share_cols]
        shares = shares.reshape(groups, row_block, held, share_cols)
        shares = jnp.moveaxis(shares, 2, 1).reshape(groups * held, row_block, share_cols)
        their_asks = stage_one[:, 0, held * share_cols : held * share_cols + 2].astype(jnp.int32)
        their_pages = their_asks[:, 0]
        their_adapters = their_asks[:, 1]
        picked = jnp.take(shares, their_adapters, axis=0)
        pages = jnp.take(prefix_page_store, their_pages, axis=0).reshape(groups, row_block, -1)
        stage_two = jnp.concatenate([picked, pages], axis=2)
        stage_two = lax.all_to_all(stage_two, "req", split_axis=0, concat_axis=0, tiled=True)
        down_projected_rows = stage_two[:, :, :down_cols].reshape(down_shape)
        up_projected_rows = stage_two[:, :, down_cols:share_cols].reshape(up_shape)
        fetched = stage_two[:, :, share_cols:].reshape((groups,) + page_shape)
    else:
        parts_out = []
        for a in range(held):
            parts_out.append(to_pieces(adapter_down_weight[a, 0], groups))
            parts_out.append(to_pieces(adapter_up_weight[a, 0], groups))
        parts_out.append(asks[:, None, :])
        stage_one = jnp.concatenate(parts_out, axis=1)
        stage_one = lax.all_to_all(stage_one, "req", split_axis=0, concat_axis=0, tiled=True)
        share_rows = down_rows + up_rows
        shares = stage_one[:, : held * share_rows].reshape(groups * held, share_rows, LANES)
        their_asks = stage_one[:, held * share_rows, :2].astype(jnp.int32)
        their_pages = their_asks[:, 0]
        their_adapters = their_asks[:, 1]
        picked = jnp.take(shares, their_adapters, axis=0)
        pages = jnp.take(prefix_page_store, their_pages, axis=0)
        page_pieces = jax.vmap(lambda page: to_pieces(page, 1)[0])(pages)
        stage_two = jnp.concatenate([picked, page_pieces], axis=1)
        stage_two = lax.all_to_all(stage_two, "req", split_axis=0, concat_axis=0, tiled=True)
        down_projected_rows = from_pieces(stage_two[:, :down_rows], down_shape)
        up_projected_rows = from_pieces(stage_two[:, down_rows:share_rows], up_shape)
        fetched = jax.vmap(lambda piece: from_pieces(piece[None], page_shape))(
            stage_two[:, share_rows:]
        )

    partial_value = lax.dot_general(
        hidden, down_projected_rows, (((1,), (1,)), ((), ())), preferred_element_type=jnp.float32
    )
    mp_count = lax.axis_size("mp")
    if mp_count == 2:
        partner = lax.ppermute(partial_value, "mp", [(0, 1), (1, 0)])
        rank_reduce = (partial_value + partner).astype(jnp.bfloat16)
    else:
        rank_reduce = lax.psum(partial_value, "mp").astype(jnp.bfloat16)
    adapter_delta = jnp.dot(rank_reduce, up_projected_rows, preferred_element_type=jnp.float32)
    query_head_count = base_query_block.shape[1] // head_width
    positions = page_len * page_count + jnp.arange(total_row_count, dtype=jnp.int32)
    reduced_sum = (base_query_block.astype(jnp.float32) + adapter_delta).reshape(
        total_row_count, query_head_count, head_width
    )
    queries = rotate(reduced_sum, positions).astype(jnp.bfloat16)
    block_keys = rotate(key_value_block[:, None, :head_width].astype(jnp.float32), positions)[
        :, 0
    ].astype(jnp.bfloat16)
    flat_pages = fetched.reshape(groups * page_len, 2 * head_width)
    prefix_mask = jnp.repeat(wanted >= 0, page_len)
    all_keys = jnp.concatenate([flat_pages[:, :head_width], block_keys], axis=0)
    all_values = jnp.concatenate(
        [flat_pages[:, head_width:], key_value_block[:, head_width:]], axis=0
    )
    token_order = jnp.arange(total_row_count, dtype=jnp.int32)
    causal = token_order[:, None] >= token_order[None, :]
    allowed = jnp.concatenate(
        [
            jnp.broadcast_to(prefix_mask[None, :], (total_row_count, groups * page_len)),
            causal,
        ],
        axis=1,
    )
    return attend(queries, all_keys, all_values, allowed)


def solution(mesh):
    in_specs = (
        P(("parts", "req"), "mp"),
        P(("parts", "req"), "mp"),
        P(("parts", "req"), None),
        P(("parts", "req"), None, None),
        P("req", "mp", None, None),
        P("req", "mp", None, None),
        P(("parts", "req")),
        P(("parts", "req")),
        P(("parts", "req"), None),
        P(("parts", "req"), None),
    )
    out_specs = P(("parts", "req"), "mp")
    return jax.shard_map(
        on_device, mesh=mesh, in_specs=in_specs, out_specs=out_specs, check_vma=False
    )
```

```python
import math

import jax
import jax.numpy as jnp
from jax import lax
from jax.experimental import pallas as pl
from jax.experimental.pallas import tpu as pltpu
from jax.sharding import PartitionSpec as P

ROPE_BASE = 500000.0
LANES = 128
TILE_ROWS = 8


def rotate(vectors, positions):
    head_width = vectors.shape[-1]
    half_dim = head_width // 2
    frequency = ROPE_BASE ** (-2.0 * jnp.arange(half_dim, dtype=jnp.float32) / head_width)
    angles = positions.astype(jnp.float32)[:, None] * frequency[None, :]
    cosine = jnp.concatenate([jnp.cos(angles), jnp.cos(angles)], axis=1)[:, None, :]
    sine_part = jnp.concatenate([jnp.sin(angles), jnp.sin(angles)], axis=1)[:, None, :]
    turned = jnp.concatenate([-vectors[..., half_dim:], vectors[..., :half_dim]], axis=-1)
    return vectors * cosine + turned * sine_part


def pack_kernel(*refs):
    *sources, out_ref, sems = refs
    copies = []
    start = 0
    for index, source in enumerate(sources):
        width = source.shape[2]
        copies.append(
            pltpu.make_async_copy(
                source, out_ref.at[:, :, pl.ds(start, width)], sems.at[index]
            )
        )
        start += width
    for copy in copies:
        copy.start()
    for copy in copies:
        copy.wait()


def pack_lanes(sources):
    lead = sources[0].shape[:2]
    width = sum(source.shape[2] for source in sources)
    return pl.pallas_call(
        pack_kernel,
        out_shape=jax.ShapeDtypeStruct(lead + (width,), sources[0].dtype),
        in_specs=[pl.BlockSpec(memory_space=pl.ANY)] * len(sources),
        out_specs=pl.BlockSpec(memory_space=pl.ANY),
        scratch_shapes=[pltpu.SemaphoreType.DMA((len(sources),))],
    )(*sources)


def tiled_ok(shape, groups):
    rows, cols = shape
    if rows % TILE_ROWS or cols % LANES:
        return False
    return ((rows // TILE_ROWS) * (cols // LANES)) % groups == 0


def to_pieces(matrix, groups):
    rows, cols = matrix.shape
    if tiled_ok(matrix.shape, groups):
        tiles = matrix.reshape(rows // TILE_ROWS, TILE_ROWS, cols // LANES, LANES)
        tiles = jnp.transpose(tiles, (0, 2, 1, 3))
        return tiles.reshape(groups, -1, LANES)
    flat = matrix.reshape(groups, -1)
    extra = (-flat.shape[1]) % LANES
    if extra:
        flat = jnp.pad(flat, ((0, 0), (0, extra)))
    return flat.reshape(groups, -1, LANES)


def from_pieces(pieces, shape):
    rows, cols = shape
    groups = pieces.shape[0]
    if tiled_ok(shape, groups):
        tiles = pieces.reshape(rows // TILE_ROWS, cols // LANES, TILE_ROWS, LANES)
        tiles = jnp.transpose(tiles, (0, 2, 1, 3))
        return tiles.reshape(rows, cols)
    flat = pieces.reshape(groups, -1)[:, : rows * cols // groups]
    return flat.reshape(rows, cols)


def piece_rows(shape, groups):
    rows, cols = shape
    if tiled_ok(shape, groups):
        return rows * cols // groups // LANES
    return -(-(rows * cols // groups) // LANES)


def attend(queries, all_keys, all_values, allowed):
    token_count, head_count, head_width = queries.shape
    score_scale = 1.0 / math.sqrt(head_width)
    rows = queries.reshape(token_count * head_count, head_width)
    scores = (
        lax.dot_general(
            rows, all_keys, (((1,), (1,)), ((), ())), preferred_element_type=jnp.float32
        )
        * score_scale
    )
    scores = scores.reshape(token_count, head_count, -1)
    scores = jnp.where(allowed[:, None, :], scores, -jnp.inf)
    row_max = jnp.max(scores, axis=2, keepdims=True)
    weights = jnp.exp(scores - row_max)
    weights_bf = (weights / jnp.sum(weights, axis=2, keepdims=True)).astype(jnp.bfloat16)
    out = jnp.dot(
        weights_bf.reshape(token_count * head_count, -1),
        all_values,
        preferred_element_type=jnp.float32,
    ).astype(jnp.bfloat16)
    return out.reshape(token_count, head_count * head_width)


def on_device(
    hidden,
    base_query_block,
    key_value_block,
    prefix_page_store,
    adapter_down_weight,
    adapter_up_weight,
    request_adapter,
    prefix_page_count,
    page_owner_groups,
    page_pool_row,
):
    groups = lax.axis_size("req")
    head_width = key_value_block.shape[1] // 2
    total_row_count = hidden.shape[0]
    page_len = prefix_page_store.shape[1]
    held = adapter_down_weight.shape[0]
    down_shape = adapter_down_weight.shape[2:]
    up_shape = adapter_up_weight.shape[2:]
    down_rows = piece_rows(down_shape, groups)
    up_rows = piece_rows(up_shape, groups)

    page_count = prefix_page_count[0]
    slot_order = jnp.arange(page_owner_groups.shape[1], dtype=jnp.int32)
    live_slots = slot_order < page_count
    holder_order = jnp.arange(groups, dtype=jnp.int32)
    matched = (page_owner_groups[0][None, :] == holder_order[:, None]) & live_slots[None, :]
    wanted = jnp.max(jnp.where(matched, page_pool_row[0][None, :], -1), axis=1)

    page_shape = prefix_page_store.shape[1:]
    row_block = down_shape[0] // groups if down_shape[0] % groups == 0 else 0
    fast = (
        row_block > 0
        and row_block % TILE_ROWS == 0
        and up_shape[0] == down_shape[0]
        and (page_shape[0] * page_shape[1]) % (row_block * LANES) == 0
    )
    lane = lax.broadcasted_iota(jnp.int32, (groups, LANES), 1)
    asks = jnp.where(
        lane == 0,
        jnp.maximum(wanted, 0)[:, None],
        jnp.where(lane == 1, request_adapter[0], 0),
    ).astype(jnp.bfloat16)

    if fast:
        down_cols = down_shape[1]
        share_cols = down_cols + up_shape[1]
        ask_rows = jnp.broadcast_to(asks[:, None, :], (groups, row_block, LANES))
        parts_out = []
        for a in range(held):
            parts_out.append(adapter_down_weight[a, 0].reshape(groups, row_block, -1))
            parts_out.append(adapter_up_weight[a, 0].reshape(groups, row_block, -1))
        parts_out.append(ask_rows)
        stage_one = pack_lanes(parts_out)
        stage_one = lax.all_to_all(stage_one, "req", split_axis=0, concat_axis=0, tiled=True)
        shares = stage_one[:, :, : held * share_cols]
        shares = shares.reshape(groups, row_block, held, share_cols)
        shares = jnp.moveaxis(shares, 2, 1).reshape(groups * held, row_block, share_cols)
        their_asks = stage_one[:, 0, held * share_cols : held * share_cols + 2].astype(jnp.int32)
        their_pages = their_asks[:, 0]
        their_adapters = their_asks[:, 1]
        picked = jnp.take(shares, their_adapters, axis=0, mode="clip")
        pages = jnp.take(prefix_page_store, their_pages, axis=0, mode="clip").reshape(groups, row_block, -1)
        stage_two = jnp.concatenate([picked, pages], axis=2)
        stage_two = lax.all_to_all(stage_two, "req", split_axis=0, concat_axis=0, tiled=True)
        down_projected_rows = stage_two[:, :, :down_cols].reshape(down_shape)
        up_projected_rows = stage_two[:, :, down_cols:share_cols].reshape(up_shape)
        fetched = stage_two[:, :, share_cols:].reshape((groups,) + page_shape)
    else:
        parts_out = []
        for a in range(held):
            parts_out.append(to_pieces(adapter_down_weight[a, 0], groups))
            parts_out.append(to_pieces(adapter_up_weight[a, 0], groups))
        parts_out.append(asks[:, None, :])
        stage_one = jnp.concatenate(parts_out, axis=1)
        stage_one = lax.all_to_all(stage_one, "req", split_axis=0, concat_axis=0, tiled=True)
        share_rows = down_rows + up_rows
        shares = stage_one[:, : held * share_rows].reshape(groups * held, share_rows, LANES)
        their_asks = stage_one[:, held * share_rows, :2].astype(jnp.int32)
        their_pages = their_asks[:, 0]
        their_adapters = their_asks[:, 1]
        picked = jnp.take(shares, their_adapters, axis=0, mode="clip")
        pages = jnp.take(prefix_page_store, their_pages, axis=0, mode="clip")
        page_pieces = jax.vmap(lambda page: to_pieces(page, 1)[0])(pages)
        stage_two = jnp.concatenate([picked, page_pieces], axis=1)
        stage_two = lax.all_to_all(stage_two, "req", split_axis=0, concat_axis=0, tiled=True)
        down_projected_rows = from_pieces(stage_two[:, :down_rows], down_shape)
        up_projected_rows = from_pieces(stage_two[:, down_rows:share_rows], up_shape)
        fetched = jax.vmap(lambda piece: from_pieces(piece[None], page_shape))(
            stage_two[:, share_rows:]
        )

    partial_value = lax.dot_general(
        hidden, down_projected_rows, (((1,), (1,)), ((), ())), preferred_element_type=jnp.float32
    )
    mp_count = lax.axis_size("mp")
    if mp_count == 2:
        partner = lax.ppermute(partial_value, "mp", [(0, 1), (1, 0)])
        rank_reduce = (partial_value + partner).astype(jnp.bfloat16)
    else:
        rank_reduce = lax.psum(partial_value, "mp").astype(jnp.bfloat16)
    adapter_delta = jnp.dot(rank_reduce, up_projected_rows, preferred_element_type=jnp.float32)
    query_head_count = base_query_block.shape[1] // head_width
    positions = page_len * page_count + jnp.arange(total_row_count, dtype=jnp.int32)
    reduced_sum = (base_query_block.astype(jnp.float32) + adapter_delta).reshape(
        total_row_count, query_head_count, head_width
    )
    queries = rotate(reduced_sum, positions).astype(jnp.bfloat16)
    block_keys = rotate(key_value_block[:, None, :head_width].astype(jnp.float32), positions)[
        :, 0
    ].astype(jnp.bfloat16)
    flat_pages = fetched.reshape(groups * page_len, 2 * head_width)
    prefix_mask = jnp.repeat(wanted >= 0, page_len)
    all_keys = jnp.concatenate([flat_pages[:, :head_width], block_keys], axis=0)
    all_values = jnp.concatenate(
        [flat_pages[:, head_width:], key_value_block[:, head_width:]], axis=0
    )
    token_order = jnp.arange(total_row_count, dtype=jnp.int32)
    causal = token_order[:, None] >= token_order[None, :]
    allowed = jnp.concatenate(
        [
            jnp.broadcast_to(prefix_mask[None, :], (total_row_count, groups * page_len)),
            causal,
        ],
        axis=1,
    )
    return attend(queries, all_keys, all_values, allowed)


def solution(mesh):
    in_specs = (
        P(("parts", "req"), "mp"),
        P(("parts", "req"), "mp"),
        P(("parts", "req"), None),
        P(("parts", "req"), None, None),
        P("req", "mp", None, None),
        P("req", "mp", None, None),
        P(("parts", "req")),
        P(("parts", "req")),
        P(("parts", "req"), None),
        P(("parts", "req"), None),
    )
    out_specs = P(("parts", "req"), "mp")
    return jax.shard_map(
        on_device, mesh=mesh, in_specs=in_specs, out_specs=out_specs, check_vma=False
    )
```

```python
import math

import jax
import jax.numpy as jnp
from jax import lax
from jax.sharding import PartitionSpec as P

ROPE_BASE = 500000.0
LANES = 128
TILE_ROWS = 8


def rotate(vectors, positions):
    head_width = vectors.shape[-1]
    half_dim = head_width // 2
    frequency = ROPE_BASE ** (-2.0 * jnp.arange(half_dim, dtype=jnp.float32) / head_width)
    angles = positions.astype(jnp.float32)[:, None] * frequency[None, :]
    cosine = jnp.concatenate([jnp.cos(angles), jnp.cos(angles)], axis=1)[:, None, :]
    sine_part = jnp.concatenate([jnp.sin(angles), jnp.sin(angles)], axis=1)[:, None, :]
    turned = jnp.concatenate([-vectors[..., half_dim:], vectors[..., :half_dim]], axis=-1)
    return vectors * cosine + turned * sine_part


def tiled_ok(shape, groups):
    rows, cols = shape
    if rows % TILE_ROWS or cols % LANES:
        return False
    return ((rows // TILE_ROWS) * (cols // LANES)) % groups == 0


def to_pieces(matrix, groups):
    rows, cols = matrix.shape
    if tiled_ok(matrix.shape, groups):
        tiles = matrix.reshape(rows // TILE_ROWS, TILE_ROWS, cols // LANES, LANES)
        tiles = jnp.transpose(tiles, (0, 2, 1, 3))
        return tiles.reshape(groups, -1, LANES)
    flat = matrix.reshape(groups, -1)
    extra = (-flat.shape[1]) % LANES
    if extra:
        flat = jnp.pad(flat, ((0, 0), (0, extra)))
    return flat.reshape(groups, -1, LANES)


def from_pieces(pieces, shape):
    rows, cols = shape
    groups = pieces.shape[0]
    if tiled_ok(shape, groups):
        tiles = pieces.reshape(rows // TILE_ROWS, cols // LANES, TILE_ROWS, LANES)
        tiles = jnp.transpose(tiles, (0, 2, 1, 3))
        return tiles.reshape(rows, cols)
    flat = pieces.reshape(groups, -1)[:, : rows * cols // groups]
    return flat.reshape(rows, cols)


def piece_rows(shape, groups):
    rows, cols = shape
    if tiled_ok(shape, groups):
        return rows * cols // groups // LANES
    return -(-(rows * cols // groups) // LANES)


def attend(queries, all_keys, all_values, allowed):
    token_count, head_count, head_width = queries.shape
    score_scale = 1.0 / math.sqrt(head_width)
    rows = queries.reshape(token_count * head_count, head_width)
    scores = (
        lax.dot_general(
            rows, all_keys, (((1,), (1,)), ((), ())), preferred_element_type=jnp.float32
        )
        * score_scale
    )
    scores = scores.reshape(token_count, head_count, -1)
    scores = jnp.where(allowed[:, None, :], scores, -jnp.inf)
    row_max = jnp.max(scores, axis=2, keepdims=True)
    weights = jnp.exp(scores - row_max)
    weights_bf = (weights / jnp.sum(weights, axis=2, keepdims=True)).astype(jnp.bfloat16)
    out = jnp.dot(
        weights_bf.reshape(token_count * head_count, -1),
        all_values,
        preferred_element_type=jnp.float32,
    ).astype(jnp.bfloat16)
    return out.reshape(token_count, head_count * head_width)


def on_device(
    hidden,
    base_query_block,
    key_value_block,
    prefix_page_store,
    adapter_down_weight,
    adapter_up_weight,
    request_adapter,
    prefix_page_count,
    page_owner_groups,
    page_pool_row,
):
    groups = lax.axis_size("req")
    head_width = key_value_block.shape[1] // 2
    total_row_count = hidden.shape[0]
    page_len = prefix_page_store.shape[1]
    held = adapter_down_weight.shape[0]
    down_shape = adapter_down_weight.shape[2:]
    up_shape = adapter_up_weight.shape[2:]
    down_rows = piece_rows(down_shape, groups)
    up_rows = piece_rows(up_shape, groups)

    page_count = prefix_page_count[0]
    slot_order = jnp.arange(page_owner_groups.shape[1], dtype=jnp.int32)
    live_slots = slot_order < page_count
    holder_order = jnp.arange(groups, dtype=jnp.int32)
    matched = (page_owner_groups[0][None, :] == holder_order[:, None]) & live_slots[None, :]
    wanted = jnp.max(jnp.where(matched, page_pool_row[0][None, :], -1), axis=1)

    page_shape = prefix_page_store.shape[1:]
    row_block = down_shape[0] // groups if down_shape[0] % groups == 0 else 0
    fast = (
        row_block > 0
        and row_block % TILE_ROWS == 0
        and up_shape[0] == down_shape[0]
        and (page_shape[0] * page_shape[1]) % (row_block * LANES) == 0
    )
    split_pages = (
        fast
        and lax.axis_size("mp") == 2
        and page_shape[0] % 2 == 0
        and (page_shape[0] // 2 * page_shape[1]) % (row_block * LANES) == 0
    )
    lane = lax.broadcasted_iota(jnp.int32, (groups, LANES), 1)
    asks = jnp.where(
        lane == 0,
        jnp.maximum(wanted, 0)[:, None],
        jnp.where(lane == 1, request_adapter[0], 0),
    ).astype(jnp.bfloat16)

    if fast:
        down_cols = down_shape[1]
        share_cols = down_cols + up_shape[1]
        ask_rows = jnp.broadcast_to(asks[:, None, :], (groups, row_block, LANES))
        parts_out = []
        for a in range(held):
            parts_out.append(adapter_down_weight[a, 0].reshape(groups, row_block, -1))
            parts_out.append(adapter_up_weight[a, 0].reshape(groups, row_block, -1))
        parts_out.append(ask_rows)
        stage_one = jnp.concatenate(parts_out, axis=2)
        stage_one = lax.all_to_all(stage_one, "req", split_axis=0, concat_axis=0, tiled=True)
        shares = stage_one[:, :, : held * share_cols]
        shares = shares.reshape(groups, row_block, held, share_cols)
        shares = jnp.moveaxis(shares, 2, 1).reshape(groups * held, row_block, share_cols)
        their_asks = stage_one[:, 0, held * share_cols : held * share_cols + 2].astype(jnp.int32)
        their_pages = their_asks[:, 0]
        their_adapters = their_asks[:, 1]
        picked = jnp.take(shares, their_adapters, axis=0, mode="clip")
        pages = jnp.take(prefix_page_store, their_pages, axis=0, mode="clip")
        if split_pages:
            half_rows = page_shape[0] // 2
            pages = lax.dynamic_slice_in_dim(pages, lax.axis_index("mp") * half_rows, half_rows, 1)
        stage_two = jnp.concatenate([picked, pages.reshape(groups, row_block, -1)], axis=2)
        stage_two = lax.all_to_all(stage_two, "req", split_axis=0, concat_axis=0, tiled=True)
        down_projected_rows = stage_two[:, :, :down_cols].reshape(down_shape)
        up_projected_rows = stage_two[:, :, down_cols:share_cols].reshape(up_shape)
        if split_pages:
            mine = stage_two[:, :, share_cols:].reshape(groups, half_rows, page_shape[1])
            other = lax.ppermute(mine, "mp", [(0, 1), (1, 0)])
            fetched = jnp.concatenate([mine, other], axis=1)
        else:
            fetched = stage_two[:, :, share_cols:].reshape((groups,) + page_shape)
    else:
        parts_out = []
        for a in range(held):
            parts_out.append(to_pieces(adapter_down_weight[a, 0], groups))
            parts_out.append(to_pieces(adapter_up_weight[a, 0], groups))
        parts_out.append(asks[:, None, :])
        stage_one = jnp.concatenate(parts_out, axis=1)
        stage_one = lax.all_to_all(stage_one, "req", split_axis=0, concat_axis=0, tiled=True)
        share_rows = down_rows + up_rows
        shares = stage_one[:, : held * share_rows].reshape(groups * held, share_rows, LANES)
        their_asks = stage_one[:, held * share_rows, :2].astype(jnp.int32)
        their_pages = their_asks[:, 0]
        their_adapters = their_asks[:, 1]
        picked = jnp.take(shares, their_adapters, axis=0, mode="clip")
        pages = jnp.take(prefix_page_store, their_pages, axis=0, mode="clip")
        page_pieces = jax.vmap(lambda page: to_pieces(page, 1)[0])(pages)
        stage_two = jnp.concatenate([picked, page_pieces], axis=1)
        stage_two = lax.all_to_all(stage_two, "req", split_axis=0, concat_axis=0, tiled=True)
        down_projected_rows = from_pieces(stage_two[:, :down_rows], down_shape)
        up_projected_rows = from_pieces(stage_two[:, down_rows:share_rows], up_shape)
        fetched = jax.vmap(lambda piece: from_pieces(piece[None], page_shape))(
            stage_two[:, share_rows:]
        )

    partial_value = lax.dot_general(
        hidden, down_projected_rows, (((1,), (1,)), ((), ())), preferred_element_type=jnp.float32
    )
    mp_count = lax.axis_size("mp")
    if mp_count == 2:
        partner = lax.ppermute(partial_value, "mp", [(0, 1), (1, 0)])
        rank_reduce = (partial_value + partner).astype(jnp.bfloat16)
    else:
        rank_reduce = lax.psum(partial_value, "mp").astype(jnp.bfloat16)
    adapter_delta = jnp.dot(rank_reduce, up_projected_rows, preferred_element_type=jnp.float32)
    query_head_count = base_query_block.shape[1] // head_width
    positions = page_len * page_count + jnp.arange(total_row_count, dtype=jnp.int32)
    reduced_sum = (base_query_block.astype(jnp.float32) + adapter_delta).reshape(
        total_row_count, query_head_count, head_width
    )
    queries = rotate(reduced_sum, positions).astype(jnp.bfloat16)
    block_keys = rotate(key_value_block[:, None, :head_width].astype(jnp.float32), positions)[
        :, 0
    ].astype(jnp.bfloat16)
    flat_pages = fetched.reshape(groups * page_len, 2 * head_width)
    prefix_mask = jnp.repeat(wanted >= 0, page_len)
    all_keys = jnp.concatenate([flat_pages[:, :head_width], block_keys], axis=0)
    all_values = jnp.concatenate(
        [flat_pages[:, head_width:], key_value_block[:, head_width:]], axis=0
    )
    token_order = jnp.arange(total_row_count, dtype=jnp.int32)
    causal = token_order[:, None] >= token_order[None, :]
    allowed = jnp.concatenate(
        [
            jnp.broadcast_to(prefix_mask[None, :], (total_row_count, groups * page_len)),
            causal,
        ],
        axis=1,
    )
    return attend(queries, all_keys, all_values, allowed)


def solution(mesh):
    in_specs = (
        P(("parts", "req"), "mp"),
        P(("parts", "req"), "mp"),
        P(("parts", "req"), None),
        P(("parts", "req"), None, None),
        P("req", "mp", None, None),
        P("req", "mp", None, None),
        P(("parts", "req")),
        P(("parts", "req")),
        P(("parts", "req"), None),
        P(("parts", "req"), None),
    )
    out_specs = P(("parts", "req"), "mp")
    return jax.shard_map(
        on_device, mesh=mesh, in_specs=in_specs, out_specs=out_specs, check_vma=False
    )
```

```python
import math

import jax
import jax.numpy as jnp
from jax import lax
from jax.sharding import PartitionSpec as P

ROPE_BASE = 500000.0
LANES = 128
TILE_ROWS = 8


def rotate(vectors, positions):
    head_width = vectors.shape[-1]
    half_dim = head_width // 2
    frequency = ROPE_BASE ** (-2.0 * jnp.arange(half_dim, dtype=jnp.float32) / head_width)
    angles = positions.astype(jnp.float32)[:, None] * frequency[None, :]
    cosine = jnp.concatenate([jnp.cos(angles), jnp.cos(angles)], axis=1)[:, None, :]
    sine_part = jnp.concatenate([jnp.sin(angles), jnp.sin(angles)], axis=1)[:, None, :]
    turned = jnp.concatenate([-vectors[..., half_dim:], vectors[..., :half_dim]], axis=-1)
    return vectors * cosine + turned * sine_part


def tiled_ok(shape, groups):
    rows, cols = shape
    if rows % TILE_ROWS or cols % LANES:
        return False
    return ((rows // TILE_ROWS) * (cols // LANES)) % groups == 0


def to_pieces(matrix, groups):
    rows, cols = matrix.shape
    if tiled_ok(matrix.shape, groups):
        tiles = matrix.reshape(rows // TILE_ROWS, TILE_ROWS, cols // LANES, LANES)
        tiles = jnp.transpose(tiles, (0, 2, 1, 3))
        return tiles.reshape(groups, -1, LANES)
    flat = matrix.reshape(groups, -1)
    extra = (-flat.shape[1]) % LANES
    if extra:
        flat = jnp.pad(flat, ((0, 0), (0, extra)))
    return flat.reshape(groups, -1, LANES)


def from_pieces(pieces, shape):
    rows, cols = shape
    groups = pieces.shape[0]
    if tiled_ok(shape, groups):
        tiles = pieces.reshape(rows // TILE_ROWS, cols // LANES, TILE_ROWS, LANES)
        tiles = jnp.transpose(tiles, (0, 2, 1, 3))
        return tiles.reshape(rows, cols)
    flat = pieces.reshape(groups, -1)[:, : rows * cols // groups]
    return flat.reshape(rows, cols)


def piece_rows(shape, groups):
    rows, cols = shape
    if tiled_ok(shape, groups):
        return rows * cols // groups // LANES
    return -(-(rows * cols // groups) // LANES)


def attend(queries, all_keys, all_values, allowed):
    token_count, head_count, head_width = queries.shape
    score_scale = 1.0 / math.sqrt(head_width)
    rows = jnp.transpose(queries, (1, 0, 2)).reshape(head_count * token_count, head_width)
    scores = (
        lax.dot_general(
            rows, all_keys, (((1,), (1,)), ((), ())), preferred_element_type=jnp.float32
        )
        * score_scale
    )
    scores = jnp.where(jnp.tile(allowed, (head_count, 1)), scores, -jnp.inf)
    row_max = jnp.max(scores, axis=1, keepdims=True)
    weights = jnp.exp(scores - row_max)
    weights_bf = (weights / jnp.sum(weights, axis=1, keepdims=True)).astype(jnp.bfloat16)
    out = jnp.dot(weights_bf, all_values, preferred_element_type=jnp.float32).astype(
        jnp.bfloat16
    )
    out = lax.optimization_barrier(out).reshape(head_count, token_count, head_width)
    return jnp.transpose(out, (1, 0, 2)).reshape(token_count, head_count * head_width)


def on_device(
    hidden,
    base_query_block,
    key_value_block,
    prefix_page_store,
    adapter_down_weight,
    adapter_up_weight,
    request_adapter,
    prefix_page_count,
    page_owner_groups,
    page_pool_row,
):
    groups = lax.axis_size("req")
    head_width = key_value_block.shape[1] // 2
    total_row_count = hidden.shape[0]
    page_len = prefix_page_store.shape[1]
    held = adapter_down_weight.shape[0]
    down_shape = adapter_down_weight.shape[2:]
    up_shape = adapter_up_weight.shape[2:]
    down_rows = piece_rows(down_shape, groups)
    up_rows = piece_rows(up_shape, groups)

    page_count = prefix_page_count[0]
    slot_order = jnp.arange(page_owner_groups.shape[1], dtype=jnp.int32)
    live_slots = slot_order < page_count
    holder_order = jnp.arange(groups, dtype=jnp.int32)
    matched = (page_owner_groups[0][None, :] == holder_order[:, None]) & live_slots[None, :]
    wanted = jnp.max(jnp.where(matched, page_pool_row[0][None, :], -1), axis=1)

    page_shape = prefix_page_store.shape[1:]
    row_block = down_shape[0] // groups if down_shape[0] % groups == 0 else 0
    fast = (
        row_block > 0
        and row_block % TILE_ROWS == 0
        and up_shape[0] == down_shape[0]
        and (page_shape[0] * page_shape[1]) % (row_block * LANES) == 0
    )
    split_pages = (
        fast
        and lax.axis_size("mp") == 2
        and page_shape[0] % 2 == 0
        and (page_shape[0] // 2 * page_shape[1]) % (row_block * LANES) == 0
    )
    lane = lax.broadcasted_iota(jnp.int32, (groups, LANES), 1)
    asks = jnp.where(
        lane == 0,
        jnp.maximum(wanted, 0)[:, None],
        jnp.where(lane == 1, request_adapter[0], 0),
    ).astype(jnp.bfloat16)

    if fast:
        down_cols = down_shape[1]
        share_cols = down_cols + up_shape[1]
        ask_rows = jnp.broadcast_to(asks[:, None, :], (groups, row_block, LANES))
        parts_out = []
        for a in range(held):
            parts_out.append(adapter_down_weight[a, 0].reshape(groups, row_block, -1))
            parts_out.append(adapter_up_weight[a, 0].reshape(groups, row_block, -1))
        parts_out.append(ask_rows)
        stage_one = jnp.concatenate(parts_out, axis=2)
        stage_one = lax.all_to_all(stage_one, "req", split_axis=0, concat_axis=0, tiled=True)
        shares = stage_one[:, :, : held * share_cols]
        shares = shares.reshape(groups, row_block, held, share_cols)
        shares = jnp.moveaxis(shares, 2, 1).reshape(groups * held, row_block, share_cols)
        their_asks = stage_one[:, 0, held * share_cols : held * share_cols + 2].astype(jnp.int32)
        their_pages = their_asks[:, 0]
        their_adapters = their_asks[:, 1]
        picked = jnp.take(shares, their_adapters, axis=0, mode="clip")
        pages = jnp.take(prefix_page_store, their_pages, axis=0, mode="clip")
        if split_pages:
            half_rows = page_shape[0] // 2
            pages = lax.dynamic_slice_in_dim(pages, lax.axis_index("mp") * half_rows, half_rows, 1)
        stage_two = jnp.concatenate([picked, pages.reshape(groups, row_block, -1)], axis=2)
        stage_two = lax.all_to_all(stage_two, "req", split_axis=0, concat_axis=0, tiled=True)
        down_projected_rows = stage_two[:, :, :down_cols].reshape(down_shape)
        up_projected_rows = stage_two[:, :, down_cols:share_cols].reshape(up_shape)
        if split_pages:
            mine = stage_two[:, :, share_cols:].reshape(groups, half_rows, page_shape[1])
            other = lax.ppermute(mine, "mp", [(0, 1), (1, 0)])
            fetched = jnp.concatenate([mine, other], axis=1)
        else:
            fetched = stage_two[:, :, share_cols:].reshape((groups,) + page_shape)
    else:
        parts_out = []
        for a in range(held):
            parts_out.append(to_pieces(adapter_down_weight[a, 0], groups))
            parts_out.append(to_pieces(adapter_up_weight[a, 0], groups))
        parts_out.append(asks[:, None, :])
        stage_one = jnp.concatenate(parts_out, axis=1)
        stage_one = lax.all_to_all(stage_one, "req", split_axis=0, concat_axis=0, tiled=True)
        share_rows = down_rows + up_rows
        shares = stage_one[:, : held * share_rows].reshape(groups * held, share_rows, LANES)
        their_asks = stage_one[:, held * share_rows, :2].astype(jnp.int32)
        their_pages = their_asks[:, 0]
        their_adapters = their_asks[:, 1]
        picked = jnp.take(shares, their_adapters, axis=0, mode="clip")
        pages = jnp.take(prefix_page_store, their_pages, axis=0, mode="clip")
        page_pieces = jax.vmap(lambda page: to_pieces(page, 1)[0])(pages)
        stage_two = jnp.concatenate([picked, page_pieces], axis=1)
        stage_two = lax.all_to_all(stage_two, "req", split_axis=0, concat_axis=0, tiled=True)
        down_projected_rows = from_pieces(stage_two[:, :down_rows], down_shape)
        up_projected_rows = from_pieces(stage_two[:, down_rows:share_rows], up_shape)
        fetched = jax.vmap(lambda piece: from_pieces(piece[None], page_shape))(
            stage_two[:, share_rows:]
        )

    partial_value = lax.dot_general(
        hidden, down_projected_rows, (((1,), (1,)), ((), ())), preferred_element_type=jnp.float32
    )
    mp_count = lax.axis_size("mp")
    if mp_count == 2:
        partner = lax.ppermute(partial_value, "mp", [(0, 1), (1, 0)])
        rank_reduce = (partial_value + partner).astype(jnp.bfloat16)
    else:
        rank_reduce = lax.psum(partial_value, "mp").astype(jnp.bfloat16)
    adapter_delta = jnp.dot(rank_reduce, up_projected_rows, preferred_element_type=jnp.float32)
    query_head_count = base_query_block.shape[1] // head_width
    positions = page_len * page_count + jnp.arange(total_row_count, dtype=jnp.int32)
    reduced_sum = (base_query_block.astype(jnp.float32) + adapter_delta).reshape(
        total_row_count, query_head_count, head_width
    )
    queries = rotate(reduced_sum, positions).astype(jnp.bfloat16)
    block_keys = rotate(key_value_block[:, None, :head_width].astype(jnp.float32), positions)[
        :, 0
    ].astype(jnp.bfloat16)
    flat_pages = fetched.reshape(groups * page_len, 2 * head_width)
    prefix_mask = jnp.repeat(wanted >= 0, page_len)
    all_keys = jnp.concatenate([flat_pages[:, :head_width], block_keys], axis=0)
    all_values = jnp.concatenate(
        [flat_pages[:, head_width:], key_value_block[:, head_width:]], axis=0
    )
    token_order = jnp.arange(total_row_count, dtype=jnp.int32)
    causal = token_order[:, None] >= token_order[None, :]
    allowed = jnp.concatenate(
        [
            jnp.broadcast_to(prefix_mask[None, :], (total_row_count, groups * page_len)),
            causal,
        ],
        axis=1,
    )
    return attend(queries, all_keys, all_values, allowed)


def solution(mesh):
    in_specs = (
        P(("parts", "req"), "mp"),
        P(("parts", "req"), "mp"),
        P(("parts", "req"), None),
        P(("parts", "req"), None, None),
        P("req", "mp", None, None),
        P("req", "mp", None, None),
        P(("parts", "req")),
        P(("parts", "req")),
        P(("parts", "req"), None),
        P(("parts", "req"), None),
    )
    out_specs = P(("parts", "req"), "mp")
    return jax.shard_map(
        on_device, mesh=mesh, in_specs=in_specs, out_specs=out_specs, check_vma=False
    )
```
